512 devices in a mesh: dp: 16 (over y_lo, x, core), mp: 32 (over z, y_hi).
Axes of the slice: x: 4, y: 4 (y_hi: 2, y_lo: 2; y = y_hi * 2 + y_lo), z: 16, core: 2. Of those that a mesh axis runs over, the one named last changes fastest.
Arguments:
- hidden_states: bfloat16 [8192, 2560], P(('dp', 'mp')), may hold values from -60 to 60
- norm_gain: float32 [2560], replicated, may hold values from 0.5 to 1.5
- head_weight: bfloat16 [2560, 65536], P(None, ('dp', 'mp')), may hold values from -64 to 64
- target_ids: int32 [8192], P(('dp', 'mp')), may hold values from 0 to 65535
- response_mask: int32 [8192], P(('dp', 'mp')), may hold values from 0 to 1, as said below
Outputs:
- token_logprob: float32 [8192], P(('dp', 'mp'))
- token_entropy: float32 [8192], P(('dp', 'mp'))
The draws below stay inside these ranges and needn't reach their ends.
Inputs may be any that keep to these rules, and one draw needn't show every extreme that they name: `response_mask`: each aligned run of 256 positions is one rollout: a prompt of 0s, then one span of 1s, then padding 0s.
All inputs are finite; a program needn't handle non-finite values.
Results may differ from the reference program's by a relative error of at most 0.0048.
Values may be sent and summed in bfloat16 or wider, within the bound.
No kernel may reach another device: no remote copies, remote signals or barrier semaphores. Data moves between devices by JAX's collectives and lax.ppermute only.
A program may use at most 64 MiB of HBM per device.

```python
import math
import jax
import jax.numpy as jnp
import numpy as np
from jax import lax

D = 2560
V = 65536
ROLLOUT = 256
TOKENS = 8192


def shared_draw(key):
    base = jax.random.fold_in(key, 11)
    key_head = jax.random.fold_in(base, 0)
    key_states = jax.random.fold_in(base, 1)
    key_pick = jax.random.fold_in(base, 4)
    key_loud = jax.random.fold_in(base, 6)
    key_dir = jax.random.fold_in(base, 7)
    key_gap = jax.random.fold_in(base, 8)
    key_small = jax.random.fold_in(base, 9)
    head = jax.random.normal(key_head, (D, V), jnp.float32) * (3.0 / math.sqrt(D))
    states = jnp.clip(jax.random.normal(key_states, (TOKENS, D), jnp.float32), -6.0, 6.0)
    loud_count = 4
    narrow = D // 8
    pairs = jax.random.permutation(key_loud, V // 2)[:loud_count].astype(jnp.int32)
    direction = jax.random.normal(key_dir, (loud_count, narrow), jnp.float32)
    direction = direction / jnp.sqrt(jnp.mean(direction * direction, axis=1, keepdims=True) + 1e-06)
    levels = 150.0 + 70.0 * jnp.arange(loud_count, dtype=jnp.float32)
    gaps = jax.random.uniform(key_gap, (loud_count,), jnp.float32, 1.0, 3.0)
    coef = levels * (math.sqrt(8.0) / D)
    even_cols = direction.T * coef[None, :]
    odd_cols = even_cols * (1.0 - gaps / levels)[None, :]
    head = head.at[:narrow, 2 * pairs].set(even_cols)
    head = head.at[:narrow, 2 * pairs + 1].set(odd_cols)
    band = jnp.where(jnp.arange(D) < narrow, 0.05, 1.0)[None, :]
    states = states * band
    small = 0.05 * jnp.clip(jax.random.normal(key_small, (TOKENS, D), jnp.float32), -6.0, 6.0)
    chosen_pair = jax.random.randint(key_pick, (TOKENS,), 0, loud_count)
    aligned = small.at[:, :narrow].add(jnp.take(direction, chosen_pair, axis=0))
    chooser = (jnp.arange(TOKENS) % 4 == 3)[:, None]
    states = jnp.where(chooser, aligned, states)
    return (jnp.clip(head, -64.0, 64.0), jnp.clip(states, -60.0, 60.0))


def draw_hidden_states(key, part):
    return shared_draw(key)[1].astype(jnp.bfloat16)


def draw_head_weight(key, part):
    return shared_draw(key)[0].astype(jnp.bfloat16)


def draw_response_mask(key, part):
    key_prompt, key_pad = jax.random.split(jax.random.fold_in(key, 5), 2)
    rollouts = TOKENS // ROLLOUT
    prompt_len = jax.random.randint(key_prompt, (rollouts,), ROLLOUT // 16, ROLLOUT // 4)
    pad_len = jax.random.randint(key_pad, (rollouts,), 0, ROLLOUT // 8)
    positions = jnp.arange(TOKENS, dtype=jnp.int32)
    owner = positions // ROLLOUT
    offset = positions % ROLLOUT
    start = jnp.take(prompt_len, owner)
    finish = ROLLOUT - jnp.take(pad_len, owner)
    return ((offset >= start) & (offset < finish)).astype(jnp.int32)


def with_ends(result, stream_key, low, largest):
    shape = result.shape
    spot = [jax.random.randint(jax.random.fold_in(stream_key, axis), (), 0, shape[axis]) for axis in range(len(shape))]
    result = result.at[tuple(spot)].set(low)
    longest = shape.index(max(shape))
    spot[longest] = (spot[longest] + 1) % shape[longest]
    return result.at[tuple(spot)].set(largest)


def rank_bounds(amount, slope):
    loads = [(1 << 20) // math.isqrt(grade ** slope) + 1 for grade in range(1, amount + 1)]
    scale = 1 + sum(loads) // (1 << 30)
    return np.cumsum(np.array([max(1, weight // scale) for weight in loads]))


def ranked(key, extent, number_of, lean):
    grid = rank_bounds(number_of, lean)
    pick = jax.random.randint(jax.random.fold_in(key, 1), extent, 0, int(grid[number_of - 1]))
    rank = jnp.searchsorted(jnp.asarray(grid, jnp.int32), pick, side="right")
    return jax.random.permutation(jax.random.fold_in(key, 2), number_of)[rank].astype(jnp.int32)


def setup_inputs(seed: int = 0) -> dict:
    streams_of = jax.random.split(jax.random.key(seed), 6)
    return {
        "hidden_states": draw_hidden_states(jax.random.fold_in(streams_of[5], 71), 0),
        "norm_gain": jnp.clip(1.0 + 0.1 * jax.random.normal(streams_of[1], (D,), jnp.float32), 0.5, 1.5),
        "head_weight": draw_head_weight(jax.random.fold_in(streams_of[5], 71), 0),
        "target_ids": with_ends(ranked(streams_of[3], (TOKENS,), V, 2), jax.random.fold_in(streams_of[3], 3), 0, V - 1).astype(jnp.int32),
        "response_mask": draw_response_mask(jax.random.fold_in(streams_of[5], 71), 0),
    }


def token_stats(block_states, block_targets, block_mask, norm_gain, head_weight):
    states = block_states.astype(jnp.float32)
    mean_square = lax.optimization_barrier(jnp.mean(states * states, axis=1, keepdims=True))
    normed = (states * lax.rsqrt(mean_square + 1e-06) * norm_gain[None, :]).astype(jnp.bfloat16)
    logits = jnp.dot(normed, head_weight, preferred_element_type=jnp.float32)
    top_logit = lax.optimization_barrier(jnp.max(logits, axis=1))
    weights = jnp.exp(logits - top_logit[:, None])
    weight_total = lax.optimization_barrier(jnp.sum(weights, axis=1))
    log_total = top_logit + jnp.log(weight_total)
    expected = lax.optimization_barrier(jnp.sum(weights * logits, axis=1)) / weight_total
    chosen = jnp.take_along_axis(logits, block_targets[:, None].astype(jnp.int32), axis=1)[:, 0]
    scored = block_mask.astype(jnp.float32)
    return ((chosen - log_total) * scored, (log_total - expected) * scored)

def reference(hidden_states, norm_gain, head_weight, target_ids, response_mask):
    block_rows = min(512, TOKENS)
    block_count = TOKENS // block_rows

    def one_block(inputs):
        return token_stats(inputs[0], inputs[1], inputs[2], norm_gain, head_weight)
    logprob, entropy = lax.map(one_block, (hidden_states.reshape(block_count, block_rows, D), target_ids.reshape(block_count, block_rows), response_mask.reshape(block_count, block_rows)))
    return (logprob.reshape(TOKENS), entropy.reshape(TOKENS))
```

```python
import jax
import jax.numpy as jnp
from jax import lax
from jax.sharding import PartitionSpec as P

id_base = 256


def local(hidden_states, norm_gain, head_weight, target_ids, response_mask):
    states = hidden_states.astype(jnp.float32)
    mean_square = jnp.mean(states * states, axis=1, keepdims=True)
    normed = (states * lax.rsqrt(mean_square + 1e-06) * norm_gain[None, :]).astype(jnp.bfloat16)
    width = normed.shape[1]
    mp_count = lax.axis_size("mp")
    mp_index = lax.axis_index("mp")
    shard_cols = head_weight.shape[1]
    send_count = normed.shape[0]
    id_high = (target_ids // id_base).astype(jnp.bfloat16)
    id_low = (target_ids % id_base).astype(jnp.bfloat16)
    packed = jnp.concatenate([normed, id_high[:, None], id_low[:, None]], axis=1)
    group = lax.all_gather(packed, "mp", axis=0, tiled=True)
    group_states = group[:, :width]
    group_targets = (
        group[:, width].astype(jnp.int32) * id_base + group[:, width + 1].astype(jnp.int32)
    )
    column_piece = lax.all_gather(head_weight, "dp", axis=1, tiled=True)
    positions = jnp.arange(column_piece.shape[1], dtype=jnp.int32)
    owners = positions // shard_cols
    column_ids = (owners * mp_count + mp_index) * shard_cols + positions % shard_cols

    logits = jnp.dot(group_states, column_piece, preferred_element_type=jnp.float32)
    top = jnp.max(logits, axis=1)
    shifted = jnp.exp(logits - top[:, None])
    total = jnp.sum(shifted, axis=1)
    moment = jnp.sum(shifted * logits, axis=1)
    hit = group_targets[:, None] == column_ids[None, :]
    chosen = jnp.sum(jnp.where(hit, logits, 0.0), axis=1)
    part_lse = top + jnp.log(total)
    part_expected = moment / total

    stats = jnp.stack([part_lse, part_expected, chosen], axis=0)
    stats = stats.reshape(3, mp_count, send_count)
    got = lax.all_to_all(stats, "mp", split_axis=1, concat_axis=1, tiled=True)
    lse_parts, expected_parts, chosen_parts = got[0], got[1], got[2]
    top_lse = jnp.max(lse_parts, axis=0)
    log_total = top_lse + jnp.log(jnp.sum(jnp.exp(lse_parts - top_lse[None, :]), axis=0))
    weights = jnp.exp(lse_parts - log_total[None, :])
    expected = jnp.sum(weights * expected_parts, axis=0)
    chosen_logit = jnp.sum(chosen_parts, axis=0)

    scored = response_mask.astype(jnp.float32)
    return ((chosen_logit - log_total) * scored, (log_total - expected) * scored)


def solution(mesh):
    return jax.shard_map(
        local,
        mesh=mesh,
        in_specs=(
            P(("dp", "mp"), None),
            P(),
            P(None, ("dp", "mp")),
            P(("dp", "mp")),
            P(("dp", "mp")),
        ),
        out_specs=(P(("dp", "mp")), P(("dp", "mp"))),
        check_vma=False,
    )
```

```python
import jax
import jax.numpy as jnp
from jax import lax
from jax.sharding import Mesh, PartitionSpec as P

id_base = 256
dp_axes = ("ylo", "x", "core")
mp_axes = ("z", "yhi")
every = dp_axes + mp_axes


def local(hidden_states, norm_gain, head_weight, target_ids, response_mask):
    states = hidden_states.astype(jnp.float32)
    mean_square = jnp.mean(states * states, axis=1, keepdims=True)
    normed = (states * lax.rsqrt(mean_square + 1e-06) * norm_gain[None, :]).astype(jnp.bfloat16)
    width = normed.shape[1]
    mp_count = lax.axis_size(mp_axes)
    mp_index = lax.axis_index(mp_axes)
    shard_cols = head_weight.shape[1]
    send_count = normed.shape[0]
    id_high = (target_ids // id_base).astype(jnp.bfloat16)
    id_low = (target_ids % id_base).astype(jnp.bfloat16)
    packed = jnp.concatenate([normed, id_high[:, None], id_low[:, None]], axis=1)
    pair = lax.all_gather(packed, "yhi", axis=0, tiled=True)
    group = lax.all_gather(pair, "z", axis=0, tiled=True)
    group_states = group[:, :width]
    group_targets = (
        group[:, width].astype(jnp.int32) * id_base + group[:, width + 1].astype(jnp.int32)
    )
    column_piece = lax.all_gather(head_weight, dp_axes, axis=1, tiled=True)
    positions = jnp.arange(column_piece.shape[1], dtype=jnp.int32)
    owners = positions // shard_cols
    column_ids = (owners * mp_count + mp_index) * shard_cols + positions % shard_cols

    logits = jnp.dot(group_states, column_piece, preferred_element_type=jnp.float32)
    top = jnp.max(logits, axis=1)
    shifted = jnp.exp(logits - top[:, None])
    total = jnp.sum(shifted, axis=1)
    moment = jnp.sum(shifted * logits, axis=1)
    hit = group_targets[:, None] == column_ids[None, :]
    chosen = jnp.sum(jnp.where(hit, logits, 0.0), axis=1)
    part_lse = top + jnp.log(total)
    part_expected = moment / total

    stats = jnp.stack([part_lse, part_expected, chosen], axis=0)
    stats = stats.reshape(3, mp_count, send_count)
    got = lax.all_to_all(stats, mp_axes, split_axis=1, concat_axis=1, tiled=True)
    lse_parts, expected_parts, chosen_parts = got[0], got[1], got[2]
    top_lse = jnp.max(lse_parts, axis=0)
    log_total = top_lse + jnp.log(jnp.sum(jnp.exp(lse_parts - top_lse[None, :]), axis=0))
    weights = jnp.exp(lse_parts - log_total[None, :])
    expected = jnp.sum(weights * expected_parts, axis=0)
    chosen_logit = jnp.sum(chosen_parts, axis=0)

    scored = response_mask.astype(jnp.float32)
    return ((chosen_logit - log_total) * scored, (log_total - expected) * scored)


def split_mesh(mesh):
    dp_size, mp_size = mesh.devices.shape
    shape = (2, dp_size // 4, 2, mp_size // 2, 2)
    return Mesh(mesh.devices.reshape(shape), every)


def solution(mesh):
    return jax.shard_map(
        local,
        mesh=split_mesh(mesh),
        in_specs=(
            P(every, None),
            P(),
            P(None, every),
            P(every),
            P(every),
        ),
        out_specs=(P(every), P(every)),
        check_vma=False,
    )
```

```python
import jax
import jax.numpy as jnp
from jax import lax
from jax.sharding import Mesh, PartitionSpec as P

id_base = 256
dp_axes = ("ylo", "x", "core")
mp_axes = ("z", "yhi")
every = dp_axes + mp_axes


def shift(value, axis, step):
    count = lax.axis_size(axis)
    return lax.ppermute(value, axis, [(i, (i + step) % count) for i in range(count)])


def local(hidden_states, norm_gain, head_weight, target_ids, response_mask):
    states = hidden_states.astype(jnp.float32)
    mean_square = jnp.mean(states * states, axis=1, keepdims=True)
    normed = (states * lax.rsqrt(mean_square + 1e-06) * norm_gain[None, :]).astype(jnp.bfloat16)
    width = normed.shape[1]
    mp_count = lax.axis_size(mp_axes)
    mp_index = lax.axis_index(mp_axes)
    shard_cols = head_weight.shape[1]
    send_count = normed.shape[0]
    id_high = (target_ids // id_base).astype(jnp.bfloat16)
    id_low = (target_ids % id_base).astype(jnp.bfloat16)
    packed = jnp.concatenate([normed, id_high[:, None], id_low[:, None]], axis=1)
    z_count = lax.axis_size("z")
    z_index = lax.axis_index("z")
    yhi_index = lax.axis_index("yhi")
    pair = jnp.concatenate([packed, shift(packed, "yhi", 1)], axis=0)
    ahead = pair
    behind = pair
    blocks = [pair]
    returning = []
    for _ in range(z_count // 2 - 1):
        ahead = shift(ahead, "z", 1)
        behind = shift(behind, "z", -1)
        blocks.append(ahead)
        returning.append(behind)
    blocks.append(shift(ahead, "z", 1))
    group = jnp.concatenate(blocks + returning[::-1], axis=0)
    group_states = group[:, :width]
    group_targets = (
        group[:, width].astype(jnp.int32) * id_base + group[:, width + 1].astype(jnp.int32)
    )
    column_piece = lax.all_gather(head_weight, dp_axes, axis=1, tiled=True)
    positions = jnp.arange(column_piece.shape[1], dtype=jnp.int32)
    owners = positions // shard_cols
    column_ids = (owners * mp_count + mp_index) * shard_cols + positions % shard_cols

    logits = jnp.dot(group_states, column_piece, preferred_element_type=jnp.float32)
    top = jnp.max(logits, axis=1)
    shifted = jnp.exp(logits - top[:, None])
    total = jnp.sum(shifted, axis=1)
    moment = jnp.sum(shifted * logits, axis=1)
    hit = group_targets[:, None] == column_ids[None, :]
    chosen = jnp.sum(jnp.where(hit, logits, 0.0), axis=1)
    part_lse = top + jnp.log(total)
    part_expected = moment / total

    stats = jnp.stack([part_lse, part_expected, chosen], axis=0)
    stats = stats.reshape(3, mp_count, send_count)
    owner = jnp.arange(mp_count, dtype=jnp.int32)
    source = ((z_index - owner // 2) % z_count) * 2 + (owner % 2 + yhi_index) % 2
    stats = jnp.take(stats, source, axis=1)
    got = lax.all_to_all(stats, mp_axes, split_axis=1, concat_axis=1, tiled=True)
    lse_parts, expected_parts, chosen_parts = got[0], got[1], got[2]
    top_lse = jnp.max(lse_parts, axis=0)
    log_total = top_lse + jnp.log(jnp.sum(jnp.exp(lse_parts - top_lse[None, :]), axis=0))
    weights = jnp.exp(lse_parts - log_total[None, :])
    expected = jnp.sum(weights * expected_parts, axis=0)
    chosen_logit = jnp.sum(chosen_parts, axis=0)

    scored = response_mask.astype(jnp.float32)
    return ((chosen_logit - log_total) * scored, (log_total - expected) * scored)


def split_mesh(mesh):
    dp_size, mp_size = mesh.devices.shape
    shape = (2, dp_size // 4, 2, mp_size // 2, 2)
    return Mesh(mesh.devices.reshape(shape), every)


def solution(mesh):
    return jax.shard_map(
        local,
        mesh=split_mesh(mesh),
        in_specs=(
            P(every, None),
            P(),
            P(None, every),
            P(every),
            P(every),
        ),
        out_specs=(P(every), P(every)),
        check_vma=False,
    )
```

```python
import jax
import jax.numpy as jnp
from jax import lax
from jax.sharding import Mesh, PartitionSpec as P

id_base = 256
dp_axes = ("ylo", "x", "core")
mp_axes = ("z", "yhi")
every = dp_axes + mp_axes


def shift(value, axis, step):
    count = lax.axis_size(axis)
    return lax.ppermute(value, axis, [(i, (i + step) % count) for i in range(count)])


def block_stats(group, column_piece, column_ids, width):
    group_states = group[:, :width]
    group_targets = (
        group[:, width].astype(jnp.int32) * id_base + group[:, width + 1].astype(jnp.int32)
    )
    logits = jnp.dot(group_states, column_piece, preferred_element_type=jnp.float32)
    top = jnp.max(logits, axis=1)
    shifted = jnp.exp(logits - top[:, None])
    total = jnp.sum(shifted, axis=1)
    moment = jnp.sum(shifted * logits, axis=1)
    hit = group_targets[:, None] == column_ids[None, :]
    chosen = jnp.sum(jnp.where(hit, logits, 0.0), axis=1)
    part_lse = top + jnp.log(total)
    part_expected = moment / total
    return jnp.stack([part_lse, part_expected, chosen], axis=0)


def local(hidden_states, norm_gain, head_weight, target_ids, response_mask):
    states = hidden_states.astype(jnp.float32)
    mean_square = jnp.mean(states * states, axis=1, keepdims=True)
    normed = (states * lax.rsqrt(mean_square + 1e-06) * norm_gain[None, :]).astype(jnp.bfloat16)
    width = normed.shape[1]
    mp_count = lax.axis_size(mp_axes)
    mp_index = lax.axis_index(mp_axes)
    shard_cols = head_weight.shape[1]
    send_count = normed.shape[0]
    id_high = (target_ids // id_base).astype(jnp.bfloat16)
    id_low = (target_ids % id_base).astype(jnp.bfloat16)
    packed = jnp.concatenate([normed, id_high[:, None], id_low[:, None]], axis=1)
    z_count = lax.axis_size("z")
    z_index = lax.axis_index("z")
    yhi_index = lax.axis_index("yhi")
    pair = jnp.concatenate([packed, shift(packed, "yhi", 1)], axis=0)
    ahead = pair
    behind = pair
    blocks = [pair]
    returning = []
    for _ in range(1, z_count // 2):
        ahead = shift(ahead, "z", 1)
        behind = shift(behind, "z", -1)
        blocks.append(ahead)
        returning.append(behind)
    blocks.append(shift(ahead, "z", 1))
    ordered = blocks + returning[::-1]
    chip_piece = lax.all_gather(head_weight, ("ylo", "x"), axis=1, tiled=True)
    other_piece = shift(chip_piece, "core", 1)
    column_piece = jnp.concatenate([chip_piece, other_piece], axis=1)
    core_index = lax.axis_index("core")
    positions = jnp.arange(column_piece.shape[1], dtype=jnp.int32)
    half = positions // chip_piece.shape[1]
    within = positions % chip_piece.shape[1]
    owners = (within // shard_cols) * 2 + (half + core_index) % 2
    column_ids = (owners * mp_count + mp_index) * shard_cols + within % shard_cols
    late = (z_count // 2 - 1, z_count // 2, z_count // 2 + 1)
    early = [k for k in range(z_count) if k not in late]
    early_stats = block_stats(
        jnp.concatenate([ordered[k] for k in early], axis=0), column_piece, column_ids, width
    )
    late_stats = block_stats(
        jnp.concatenate([ordered[k] for k in late], axis=0), column_piece, column_ids, width
    )
    block_rows = pair.shape[0]
    pieces = {}
    for i, k in enumerate(early):
        pieces[k] = early_stats[:, i * block_rows:(i + 1) * block_rows]
    for i, k in enumerate(late):
        pieces[k] = late_stats[:, i * block_rows:(i + 1) * block_rows]
    stats = jnp.concatenate([pieces[k] for k in range(z_count)], axis=1)
    stats = stats.reshape(3, mp_count, send_count)
    owner = jnp.arange(mp_count, dtype=jnp.int32)
    source = ((z_index - owner // 2) % z_count) * 2 + (owner % 2 + yhi_index) % 2
    stats = jnp.take(stats, source, axis=1)
    got = lax.all_to_all(stats, mp_axes, split_axis=1, concat_axis=1, tiled=True)
    lse_parts, expected_parts, chosen_parts = got[0], got[1], got[2]
    top_lse = jnp.max(lse_parts, axis=0)
    log_total = top_lse + jnp.log(jnp.sum(jnp.exp(lse_parts - top_lse[None, :]), axis=0))
    weights = jnp.exp(lse_parts - log_total[None, :])
    expected = jnp.sum(weights * expected_parts, axis=0)
    chosen_logit = jnp.sum(chosen_parts, axis=0)

    scored = response_mask.astype(jnp.float32)
    return ((chosen_logit - log_total) * scored, (log_total - expected) * scored)


def split_mesh(mesh):
    dp_size, mp_size = mesh.devices.shape
    shape = (2, dp_size // 4, 2, mp_size // 2, 2)
    return Mesh(mesh.devices.reshape(shape), every)


def solution(mesh):
    return jax.shard_map(
        local,
        mesh=split_mesh(mesh),
        in_specs=(
            P(every, None),
            P(),
            P(None, every),
            P(every),
            P(every),
        ),
        out_specs=(P(every), P(every)),
        check_vma=False,
    )
```

```python
import jax
import jax.numpy as jnp
from jax import lax
from jax.sharding import Mesh, PartitionSpec as P

id_base = 256
dp_axes = ("ylo", "x", "core")
mp_axes = ("z", "yhi")
every = dp_axes + mp_axes


def shift(value, axis, step):
    count = lax.axis_size(axis)
    return lax.ppermute(value, axis, [(i, (i + step) % count) for i in range(count)])


def block_stats(group, column_piece, column_ids, width):
    group_states = group[:, :width]
    group_targets = (
        group[:, width].astype(jnp.int32) * id_base + group[:, width + 1].astype(jnp.int32)
    )
    logits = jnp.dot(group_states, column_piece, preferred_element_type=jnp.float32)
    top = jnp.max(logits, axis=1)
    shifted = jnp.exp(logits - top[:, None])
    total = jnp.sum(shifted, axis=1)
    moment = jnp.sum(shifted * logits, axis=1)
    hit = group_targets[:, None] == column_ids[None, :]
    chosen = jnp.sum(jnp.where(hit, logits, 0.0), axis=1)
    part_lse = top + jnp.log(total)
    part_expected = moment / total
    return jnp.stack([part_lse, part_expected, chosen], axis=0)


def local(hidden_states, norm_gain, head_weight, target_ids, response_mask):
    states = hidden_states.astype(jnp.float32)
    mean_square = jnp.mean(states * states, axis=1, keepdims=True)
    normed = (states * lax.rsqrt(mean_square + 1e-06) * norm_gain[None, :]).astype(jnp.bfloat16)
    width = normed.shape[1]
    mp_count = lax.axis_size(mp_axes)
    mp_index = lax.axis_index(mp_axes)
    shard_cols = head_weight.shape[1]
    send_count = normed.shape[0]
    id_high = (target_ids // id_base).astype(jnp.bfloat16)
    id_low = (target_ids % id_base).astype(jnp.bfloat16)
    packed = jnp.concatenate([normed, id_high[:, None], id_low[:, None]], axis=1)
    z_count = lax.axis_size("z")
    z_index = lax.axis_index("z")
    yhi_index = lax.axis_index("yhi")
    pair = jnp.concatenate([packed, shift(packed, "yhi", 1)], axis=0)
    ahead = pair
    behind = pair
    blocks = [pair]
    returning = []
    for _ in range(z_count // 2 - 1):
        ahead = shift(ahead, "z", 1)
        behind = shift(behind, "z", -1)
        blocks.append(ahead)
        returning.append(behind)
    blocks.append(shift(ahead, "z", 1))
    ordered = blocks + returning[::-1]
    column_piece = lax.all_gather(head_weight, dp_axes, axis=1, tiled=True)
    positions = jnp.arange(column_piece.shape[1], dtype=jnp.int32)
    owners = positions // shard_cols
    column_ids = (owners * mp_count + mp_index) * shard_cols + positions % shard_cols
    late = (z_count // 2 - 1, z_count // 2, z_count // 2 + 1)
    early = [k for k in range(z_count) if k not in late]
    early_stats = block_stats(
        jnp.concatenate([ordered[k] for k in early], axis=0), column_piece, column_ids, width
    )
    late_stats = block_stats(
        jnp.concatenate([ordered[k] for k in late], axis=0), column_piece, column_ids, width
    )
    stats = jnp.concatenate([early_stats, late_stats], axis=1)
    stats = stats.reshape(3, mp_count, send_count)
    place = [0] * z_count
    for i, k in enumerate(early + list(late)):
        place[k] = i
    owner = jnp.arange(mp_count, dtype=jnp.int32)
    block = (z_index - owner // 2) % z_count
    source = jnp.asarray(place, jnp.int32)[block] * 2 + (owner % 2 + yhi_index) % 2
    stats = jnp.take(stats, source, axis=1)
    got = lax.all_to_all(stats, mp_axes, split_axis=1, concat_axis=1, tiled=True)
    lse_parts, expected_parts, chosen_parts = got[0], got[1], got[2]
    top_lse = jnp.max(lse_parts, axis=0)
    log_total = top_lse + jnp.log(jnp.sum(jnp.exp(lse_parts - top_lse[None, :]), axis=0))
    weights = jnp.exp(lse_parts - log_total[None, :])
    expected = jnp.sum(weights * expected_parts, axis=0)
    chosen_logit = jnp.sum(chosen_parts, axis=0)

    scored = response_mask.astype(jnp.float32)
    both = jnp.stack([chosen_logit - log_total, log_total - expected], axis=0) * scored[None, :]
    return (both[0], both[1])


def split_mesh(mesh):
    dp_size, mp_size = mesh.devices.shape
    shape = (2, dp_size // 4, 2, mp_size // 2, 2)
    return Mesh(mesh.devices.reshape(shape), every)


def solution(mesh):
    return jax.shard_map(
        local,
        mesh=split_mesh(mesh),
        in_specs=(
            P(every, None),
            P(),
            P(None, every),
            P(every),
            P(every),
        ),
        out_specs=(P(every), P(every)),
        check_vma=False,
    )
```

```python
import jax
import jax.numpy as jnp
from jax import lax
from jax.sharding import Mesh, PartitionSpec as P

id_base = 256
dp_axes = ("ylo", "x", "core")
mp_axes = ("z", "yhi")
every = dp_axes + mp_axes


def shift(value, axis, step):
    count = lax.axis_size(axis)
    return lax.ppermute(value, axis, [(i, (i + step) % count) for i in range(count)])


def block_stats(group, column_piece, column_ids, width):
    group_states = group[:, :width]
    group_targets = (
        group[:, width].astype(jnp.int32) * id_base + group[:, width + 1].astype(jnp.int32)
    )
    logits = jnp.dot(group_states, column_piece, preferred_element_type=jnp.float32)
    top = jnp.max(logits, axis=1)
    shifted = jnp.exp(logits - top[:, None])
    total = jnp.sum(shifted, axis=1)
    moment = jnp.sum(shifted * logits, axis=1)
    hit = group_targets[:, None] == column_ids[None, :]
    chosen = jnp.sum(jnp.where(hit, logits, 0.0), axis=1)
    part_lse = top + jnp.log(total)
    part_expected = moment / total
    return jnp.stack([part_lse, part_expected, chosen], axis=0)


def local(hidden_states, norm_gain, head_weight, target_ids, response_mask):
    states = hidden_states.astype(jnp.float32)
    mean_square = jnp.mean(states * states, axis=1, keepdims=True)
    normed = (states * lax.rsqrt(mean_square + 1e-06) * norm_gain[None, :]).astype(jnp.bfloat16)
    width = normed.shape[1]
    mp_count = lax.axis_size(mp_axes)
    mp_index = lax.axis_index(mp_axes)
    shard_cols = head_weight.shape[1]
    send_count = normed.shape[0]
    id_high = (target_ids // id_base).astype(jnp.bfloat16)
    id_low = (target_ids % id_base).astype(jnp.bfloat16)
    packed = jnp.concatenate([normed, id_high[:, None], id_low[:, None]], axis=1)
    z_count = lax.axis_size("z")
    z_index = lax.axis_index("z")
    yhi_index = lax.axis_index("yhi")
    pair = jnp.concatenate([packed, shift(packed, "yhi", 1)], axis=0)
    ahead = pair
    behind = pair
    blocks = [pair]
    returning = []
    for _ in range(z_count // 2 - 1):
        ahead = shift(ahead, "z", 1)
        behind = shift(behind, "z", -1)
        blocks.append(ahead)
        returning.append(behind)
    blocks.append(shift(ahead, "z", 1))
    ordered = blocks + returning[::-1]
    column_piece = lax.all_gather(head_weight, dp_axes, axis=1, tiled=True)
    positions = jnp.arange(column_piece.shape[1], dtype=jnp.int32)
    owners = positions // shard_cols
    column_ids = (owners * mp_count + mp_index) * shard_cols + positions % shard_cols
    late = (z_count // 2,)
    early = [k for k in range(z_count) if k not in late]
    early_stats = block_stats(
        jnp.concatenate([ordered[k] for k in early], axis=0), column_piece, column_ids, width
    )
    late_stats = block_stats(
        jnp.concatenate([ordered[k] for k in late], axis=0), column_piece, column_ids, width
    )
    block_rows = pair.shape[0]
    pieces = {}
    for i, k in enumerate(early):
        pieces[k] = early_stats[:, i * block_rows:(i + 1) * block_rows]
    for i, k in enumerate(late):
        pieces[k] = late_stats[:, i * block_rows:(i + 1) * block_rows]
    stats = jnp.concatenate([pieces[k] for k in range(z_count)], axis=1)
    stats = stats.reshape(3, mp_count, send_count)
    owner = jnp.arange(mp_count, dtype=jnp.int32)
    source = ((z_index - owner // 2) % z_count) * 2 + (owner % 2 + yhi_index) % 2
    stats = jnp.take(stats, source, axis=1)
    got = lax.all_to_all(stats, mp_axes, split_axis=1, concat_axis=1, tiled=True)
    lse_parts, expected_parts, chosen_parts = got[0], got[1], got[2]
    top_lse = jnp.max(lse_parts, axis=0)
    log_total = top_lse + jnp.log(jnp.sum(jnp.exp(lse_parts - top_lse[None, :]), axis=0))
    weights = jnp.exp(lse_parts - log_total[None, :])
    expected = jnp.sum(weights * expected_parts, axis=0)
    chosen_logit = jnp.sum(chosen_parts, axis=0)

    scored = response_mask.astype(jnp.float32)
    return ((chosen_logit - log_total) * scored, (log_total - expected) * scored)


def split_mesh(mesh):
    dp_size, mp_size = mesh.devices.shape
    shape = (2, dp_size // 4, 2, mp_size // 2, 2)
    return Mesh(mesh.devices.reshape(shape), every)


def solution(mesh):
    return jax.shard_map(
        local,
        mesh=split_mesh(mesh),
        in_specs=(
            P(every, None),
            P(),
            P(None, every),
            P(every),
            P(every),
        ),
        out_specs=(P(every), P(every)),
        check_vma=False,
    )
```
